256 devices in a mesh: aa: 32 (over z, x), ba: 8 (over y, core).
Axes of the slice: x: 4, y: 4, z: 8, core: 2. Of those that a mesh axis runs over, the one named last changes fastest.
Arguments:
- snapshots: float32 [8192, 65536], P(('aa', 'ba')), may hold values from -125 to 125
Outputs:
- factors: float32 [8, 64, 64], replicated
- pod_modes: float32 [8, 64, 65536], P(None, None, ('aa', 'ba'))
The draws below stay inside these ranges and needn't reach their ends.
All inputs are finite; a program needn't handle non-finite values.
Results may differ from the reference program's by a relative error of at most 0.000098.
Values sent between devices are 32-bit elements; how exact they have to be, the bound alone decides.
No kernel may reach another device: no remote copies, remote signals or barrier semaphores. Data moves between devices by JAX's collectives and lax.ppermute only.
A program may use at most 128 MiB of HBM per device.

```python
import math
import jax
import jax.numpy as jnp
from jax import lax

BLOCK = 256
FREQS = 8
BLOCKS = 32
TIMES = 8192
POINTS = 65536


def draw_snapshots(key, part):
    key_point = jax.random.fold_in(key, 11)
    key_block = jax.random.fold_in(key, 12)
    key_noise = jax.random.fold_in(key, 13)
    trend = 1.0 + 2.0 * jnp.arange(POINTS, dtype=jnp.float32) / POINTS
    point_scale = jnp.exp(jax.random.uniform(key_point, (POINTS,), jnp.float32, 0.0, math.log(10.0 / 3.0))) * trend
    block_scale = jnp.exp(jax.random.uniform(key_block, (TIMES // BLOCK,), jnp.float32, 0.0, math.log(10.0)))
    time_scale = jnp.repeat(block_scale, BLOCK)
    noise_field = jnp.clip(jax.random.normal(key_noise, (TIMES, POINTS), jnp.float32), -5.0, 5.0)
    return 0.25 * noise_field * time_scale[:, None] * point_scale[None, :]


def setup_inputs(seed: int = 0) -> dict:
    splits = jax.random.split(jax.random.key(seed), 2)
    return {
        "snapshots": draw_snapshots(jax.random.fold_in(splits[1], 71), 0),
    }


def spectral_table(block_len, points):
    sample = jnp.arange(block_len, dtype=jnp.int32)
    harmonic = jnp.arange(1, FREQS + 1, dtype=jnp.int32)
    phase_turns = (sample[:, None] * harmonic[None, :] % block_len).astype(jnp.float32) * (2.0 * math.pi / block_len)
    sample_angle = sample.astype(jnp.float32) * (2.0 * math.pi / block_len)
    window = 0.5 - 0.5 * jnp.cos(sample_angle)
    norm_scale = 1.0 / jnp.sqrt(points * jnp.sum(window * window))
    cosine = window[:, None] * jnp.cos(phase_turns) * norm_scale
    sine = -window[:, None] * jnp.sin(phase_turns) * norm_scale
    return jnp.stack([cosine, sine], axis=1)

def local_gram(spectra):
    columns = 2 * spectra.shape[0]
    product = jnp.einsum('bgfp,chfp->fbgch', spectra, spectra, precision=lax.Precision.HIGHEST)
    return product.reshape(FREQS, columns, columns)

def finish(spectra, gram_sum, points):
    blocks = spectra.shape[0]
    columns = 2 * blocks
    lower_factor = jnp.linalg.cholesky(gram_sum)
    identity = jnp.broadcast_to(jnp.eye(columns, dtype=gram_sum.dtype), lower_factor.shape)
    inverse = lax.linalg.triangular_solve(lower_factor, identity, left_side=True, lower=True)
    pod_modes = math.sqrt(points) * jnp.einsum('fibg,bgfp->fip', inverse.reshape(FREQS, columns, blocks, 2), spectra, precision=lax.Precision.HIGHEST)
    return (jnp.swapaxes(lower_factor, 1, 2), pod_modes)

def reference(snapshots):
    table = spectral_table(BLOCK, POINTS)
    arranged = snapshots.reshape(BLOCKS, BLOCK, POINTS)
    spectra = jnp.einsum('bsp,sgf->bgfp', arranged, table, precision=lax.Precision.HIGHEST)
    factors, pod_modes = finish(spectra, local_gram(spectra), POINTS)
    return (factors, pod_modes)
```

```python
import math

import jax
import jax.numpy as jnp
from jax import lax
from jax.sharding import PartitionSpec as P

FREQS = 8


def spectral_rows(block_len, points, first, count):
    sample = first + jnp.arange(count, dtype=jnp.int32)
    harmonic = jnp.arange(1, FREQS + 1, dtype=jnp.int32)
    phase_turns = (sample[:, None] * harmonic[None, :] % block_len).astype(jnp.float32) * (
        2.0 * math.pi / block_len
    )
    full = jnp.arange(block_len, dtype=jnp.int32).astype(jnp.float32) * (2.0 * math.pi / block_len)
    full_window = 0.5 - 0.5 * jnp.cos(full)
    norm_scale = 1.0 / jnp.sqrt(points * jnp.sum(full_window * full_window))
    sample_angle = sample.astype(jnp.float32) * (2.0 * math.pi / block_len)
    window = 0.5 - 0.5 * jnp.cos(sample_angle)
    cosine = window[:, None] * jnp.cos(phase_turns) * norm_scale
    sine = -window[:, None] * jnp.sin(phase_turns) * norm_scale
    return jnp.stack([cosine, sine], axis=1)


def local(snapshots):
    time_dev, points = snapshots.shape
    n_aa = lax.axis_size("aa")
    n_ba = lax.axis_size("ba")
    pts_dev = points // (n_aa * n_ba)
    block_len = time_dev * n_ba
    u = lax.axis_index("ba")
    table = spectral_rows(block_len, points, u * time_dev, time_dev)
    arranged = snapshots.reshape(time_dev, n_aa, n_ba, pts_dev)
    partial = jnp.einsum("savq,sgf->vgfaq", arranged, table, precision=lax.Precision.HIGHEST)
    block_spec = lax.psum_scatter(partial, "ba", scatter_dimension=0, tiled=True)
    spectra = lax.all_to_all(block_spec, "aa", split_axis=3, concat_axis=0, tiled=True)
    blocks = spectra.shape[0]
    columns = 2 * blocks
    cols = jnp.transpose(spectra.reshape(blocks, 2, FREQS, pts_dev), (2, 0, 1, 3)).reshape(
        FREQS, columns, pts_dev
    )
    product = jnp.einsum("fip,fjp->fij", cols, cols, precision=lax.Precision.HIGHEST)
    gram_sum = lax.psum(product, ("aa", "ba"))
    lower_factor = jnp.linalg.cholesky(gram_sum)
    identity = jnp.broadcast_to(jnp.eye(columns, dtype=gram_sum.dtype), lower_factor.shape)
    inverse = lax.linalg.triangular_solve(lower_factor, identity, left_side=True, lower=True)
    pod_modes = math.sqrt(points) * jnp.einsum(
        "fij,fjp->fip", inverse, cols, precision=lax.Precision.HIGHEST
    )
    return (jnp.swapaxes(lower_factor, 1, 2), pod_modes)


def solution(mesh):
    placed = (P(("aa", "ba"), None),)
    return jax.shard_map(
        local,
        mesh=mesh,
        in_specs=placed,
        out_specs=(P(), P(None, None, ("aa", "ba"))),
        check_vma=False,
    )
```

```python
import math

import jax
import jax.numpy as jnp
from jax import lax
from jax.sharding import PartitionSpec as P

FREQS = 8


def spectral_rows(block_len, points, first, count):
    sample = first + jnp.arange(count, dtype=jnp.int32)
    harmonic = jnp.arange(1, FREQS + 1, dtype=jnp.int32)
    phase_turns = (sample[:, None] * harmonic[None, :] % block_len).astype(jnp.float32) * (
        2.0 * math.pi / block_len
    )
    full = jnp.arange(block_len, dtype=jnp.int32).astype(jnp.float32) * (2.0 * math.pi / block_len)
    full_window = 0.5 - 0.5 * jnp.cos(full)
    norm_scale = 1.0 / jnp.sqrt(points * jnp.sum(full_window * full_window))
    sample_angle = sample.astype(jnp.float32) * (2.0 * math.pi / block_len)
    window = 0.5 - 0.5 * jnp.cos(sample_angle)
    cosine = window[:, None] * jnp.cos(phase_turns) * norm_scale
    sine = -window[:, None] * jnp.sin(phase_turns) * norm_scale
    return jnp.stack([cosine, sine], axis=1)


def all_sum(x, axes, count):
    pieces = x.reshape(count, x.size // count)
    mine = lax.all_to_all(pieces, axes, 0, 0, tiled=True).sum(0, keepdims=True)
    spread = jnp.broadcast_to(mine, pieces.shape)
    return lax.all_to_all(spread, axes, 0, 0, tiled=True).reshape(x.shape)


def local(snapshots):
    time_dev, points = snapshots.shape
    n_aa = lax.axis_size("aa")
    n_ba = lax.axis_size("ba")
    pts_dev = points // (n_aa * n_ba)
    block_len = time_dev * n_ba
    u = lax.axis_index("ba")
    table = spectral_rows(block_len, points, u * time_dev, time_dev)
    arranged = snapshots.reshape(time_dev, n_aa, n_ba, pts_dev)
    partial = jnp.einsum("savq,sgf->vgfaq", arranged, table, precision=lax.Precision.HIGHEST)
    block_spec = lax.all_to_all(partial, "ba", 0, 0, tiled=True).sum(0, keepdims=True)
    spectra = lax.all_to_all(block_spec, "aa", split_axis=3, concat_axis=0, tiled=True)
    blocks = spectra.shape[0]
    columns = 2 * blocks
    cols = jnp.transpose(spectra.reshape(blocks, 2, FREQS, pts_dev), (2, 0, 1, 3)).reshape(
        FREQS, columns, pts_dev
    )
    product = jnp.einsum("fip,fjp->fij", cols, cols, precision=lax.Precision.HIGHEST)
    gram_sum = all_sum(product, ("aa", "ba"), n_aa * n_ba)
    lower_factor = jnp.linalg.cholesky(gram_sum)
    identity = jnp.broadcast_to(jnp.eye(columns, dtype=gram_sum.dtype), lower_factor.shape)
    inverse = lax.linalg.triangular_solve(lower_factor, identity, left_side=True, lower=True)
    pod_modes = math.sqrt(points) * jnp.einsum(
        "fij,fjp->fip", inverse, cols, precision=lax.Precision.HIGHEST
    )
    return (jnp.swapaxes(lower_factor, 1, 2), pod_modes)


def solution(mesh):
    placed = (P(("aa", "ba"), None),)
    return jax.shard_map(
        local,
        mesh=mesh,
        in_specs=placed,
        out_specs=(P(), P(None, None, ("aa", "ba"))),
        check_vma=False,
    )
```

```python
import math

import jax
import jax.numpy as jnp
from jax import lax
from jax.experimental import pallas as pl
from jax.experimental.pallas import tpu as pltpu
from jax.sharding import PartitionSpec as P

FREQS = 8


def spectral_rows(block_len, points, first, count):
    sample = first + jnp.arange(count, dtype=jnp.int32)
    harmonic = jnp.arange(1, FREQS + 1, dtype=jnp.int32)
    phase_turns = (sample[:, None] * harmonic[None, :] % block_len).astype(jnp.float32) * (
        2.0 * math.pi / block_len
    )
    full = jnp.arange(block_len, dtype=jnp.int32).astype(jnp.float32) * (2.0 * math.pi / block_len)
    full_window = 0.5 - 0.5 * jnp.cos(full)
    norm_scale = 1.0 / jnp.sqrt(points * jnp.sum(full_window * full_window))
    sample_angle = sample.astype(jnp.float32) * (2.0 * math.pi / block_len)
    window = 0.5 - 0.5 * jnp.cos(sample_angle)
    cosine = window[:, None] * jnp.cos(phase_turns) * norm_scale
    sine = -window[:, None] * jnp.sin(phase_turns) * norm_scale
    return jnp.stack([cosine, sine], axis=1)


def _factor_kernel(a_ref, upper_ref, inv_ref, m_ref):
    freqs, n, _ = a_ref.shape
    rows = lax.broadcasted_iota(jnp.int32, (n, 2 * n), 0)
    lanes = lax.broadcasted_iota(jnp.int32, (n, 2 * n), 1)
    for f in range(freqs):
        m_ref[f] = jnp.concatenate([a_ref[f], (rows[:, :n] == lanes[:, :n]).astype(jnp.float32)], axis=1)

    def step(j, carry):
        for f in range(freqs):
            mf = m_ref[f]
            pivot_row = m_ref[f, pl.ds(j, 1), :]
            pivot = jnp.sum(jnp.where(lanes[:1] == j, pivot_row, 0.0), axis=1, keepdims=True)
            root = jnp.sqrt(pivot)
            new_row = pivot_row / root
            column = jnp.sum(jnp.where(lanes == j, mf, 0.0), axis=1, keepdims=True) / root
            updated = jnp.where(rows > j, mf - column * new_row, mf)
            m_ref[f] = jnp.where(rows == j, new_row, updated)
        return carry

    lax.fori_loop(0, n, step, 0)
    for f in range(freqs):
        mf = m_ref[f]
        upper_ref[f] = jnp.where(rows[:, :n] <= lanes[:, :n], mf[:, :n], 0.0)
        inv_ref[f] = mf[:, n:]

def factor(gram):
    freqs, n, _ = gram.shape
    return pl.pallas_call(
        _factor_kernel,
        out_shape=(jax.ShapeDtypeStruct(gram.shape, gram.dtype), jax.ShapeDtypeStruct(gram.shape, gram.dtype)),
        scratch_shapes=[pltpu.VMEM((freqs, n, 2 * n), jnp.float32)],
    )(gram)


def all_sum(x, axes, count):
    pieces = x.reshape(count, x.size // count)
    mine = lax.all_to_all(pieces, axes, 0, 0, tiled=True).sum(0, keepdims=True)
    spread = jnp.broadcast_to(mine, pieces.shape)
    return lax.all_to_all(spread, axes, 0, 0, tiled=True).reshape(x.shape)


def local(snapshots):
    time_dev, points = snapshots.shape
    n_aa = lax.axis_size("aa")
    n_ba = lax.axis_size("ba")
    pts_dev = points // (n_aa * n_ba)
    block_len = time_dev * n_ba
    u = lax.axis_index("ba")
    table = spectral_rows(block_len, points, u * time_dev, time_dev)
    arranged = snapshots.reshape(time_dev, n_aa, n_ba, pts_dev)
    partial = jnp.einsum("savq,sgf->vgfaq", arranged, table, precision=lax.Precision.HIGHEST)
    block_spec = lax.all_to_all(partial, "ba", 0, 0, tiled=True).sum(0, keepdims=True)
    spectra = lax.all_to_all(block_spec, "aa", split_axis=3, concat_axis=0, tiled=True)
    blocks = spectra.shape[0]
    columns = 2 * blocks
    cols = jnp.transpose(spectra.reshape(blocks, 2, FREQS, pts_dev), (2, 0, 1, 3)).reshape(
        FREQS, columns, pts_dev
    )
    product = jnp.einsum("fip,fjp->fij", cols, cols, precision=lax.Precision.HIGHEST)
    gram_sum = all_sum(product, ("aa", "ba"), n_aa * n_ba)
    upper_factor, inverse = factor(gram_sum)
    pod_modes = math.sqrt(points) * jnp.einsum(
        "fij,fjp->fip", inverse, cols, precision=lax.Precision.HIGHEST
    )
    return (upper_factor, pod_modes)


def solution(mesh):
    placed = (P(("aa", "ba"), None),)
    return jax.shard_map(
        local,
        mesh=mesh,
        in_specs=placed,
        out_specs=(P(), P(None, None, ("aa", "ba"))),
        check_vma=False,
    )
```

```python
import math

import jax
import jax.numpy as jnp
from jax import lax
from jax.experimental import pallas as pl
from jax.experimental.pallas import tpu as pltpu
from jax.sharding import PartitionSpec as P

FREQS = 8


def spectral_rows(block_len, points, first, count):
    sample = first + jnp.arange(count, dtype=jnp.int32)
    harmonic = jnp.arange(1, FREQS + 1, dtype=jnp.int32)
    phase_turns = (sample[:, None] * harmonic[None, :] % block_len).astype(jnp.float32) * (
        2.0 * math.pi / block_len
    )
    full = jnp.arange(block_len, dtype=jnp.int32).astype(jnp.float32) * (2.0 * math.pi / block_len)
    full_window = 0.5 - 0.5 * jnp.cos(full)
    norm_scale = 1.0 / jnp.sqrt(points * jnp.sum(full_window * full_window))
    sample_angle = sample.astype(jnp.float32) * (2.0 * math.pi / block_len)
    window = 0.5 - 0.5 * jnp.cos(sample_angle)
    cosine = window[:, None] * jnp.cos(phase_turns) * norm_scale
    sine = -window[:, None] * jnp.sin(phase_turns) * norm_scale
    return jnp.stack([cosine, sine], axis=1)


def _factor_kernel(a_ref, upper_ref, inv_ref, m_ref):
    freqs, n, _ = a_ref.shape
    rows = lax.broadcasted_iota(jnp.int32, (n, 2 * n), 0)
    lanes = lax.broadcasted_iota(jnp.int32, (n, 2 * n), 1)
    for f in range(freqs):
        m_ref[f] = jnp.concatenate([a_ref[f], (rows[:, :n] == lanes[:, :n]).astype(jnp.float32)], axis=1)

    def step(j, carry):
        for f in range(freqs):
            mf = m_ref[f]
            pivot_row = m_ref[f, pl.ds(j, 1), :]
            pivot = jnp.sum(jnp.where(lanes[:1] == j, pivot_row, 0.0), axis=1, keepdims=True)
            scaled_row = pivot_row / pivot
            column = jnp.sum(jnp.where(lanes == j, mf, 0.0), axis=1, keepdims=True)
            column = jnp.where(rows[:, :1] > j, column, 0.0)
            m_ref[f] = mf - column * scaled_row
            m_ref[f, pl.ds(j, 1), :] = pivot_row / jnp.sqrt(pivot)
        return carry

    lax.fori_loop(0, n, step, 0)
    for f in range(freqs):
        mf = m_ref[f]
        upper_ref[f] = jnp.where(rows[:, :n] <= lanes[:, :n], mf[:, :n], 0.0)
        inv_ref[f] = mf[:, n:]

def factor(gram):
    freqs, n, _ = gram.shape
    return pl.pallas_call(
        _factor_kernel,
        out_shape=(jax.ShapeDtypeStruct(gram.shape, gram.dtype), jax.ShapeDtypeStruct(gram.shape, gram.dtype)),
        scratch_shapes=[pltpu.VMEM((freqs, n, 2 * n), jnp.float32)],
    )(gram)


def all_sum(x, axes, count):
    pieces = x.reshape(count, x.size // count)
    mine = lax.all_to_all(pieces, axes, 0, 0, tiled=True).sum(0, keepdims=True)
    spread = jnp.broadcast_to(mine, pieces.shape)
    return lax.all_to_all(spread, axes, 0, 0, tiled=True).reshape(x.shape)


def local(snapshots):
    time_dev, points = snapshots.shape
    n_aa = lax.axis_size("aa")
    n_ba = lax.axis_size("ba")
    pts_dev = points // (n_aa * n_ba)
    block_len = time_dev * n_ba
    u = lax.axis_index("ba")
    table = spectral_rows(block_len, points, u * time_dev, time_dev)
    arranged = snapshots.reshape(time_dev, n_aa, n_ba, pts_dev)
    partial = jnp.einsum("savq,sgf->vgfaq", arranged, table, precision=lax.Precision.HIGHEST)
    block_spec = lax.all_to_all(partial, "ba", 0, 0, tiled=True).sum(0, keepdims=True)
    spectra = lax.all_to_all(block_spec, "aa", split_axis=3, concat_axis=0, tiled=True)
    blocks = spectra.shape[0]
    columns = 2 * blocks
    cols = jnp.transpose(spectra.reshape(blocks, 2, FREQS, pts_dev), (2, 0, 1, 3)).reshape(
        FREQS, columns, pts_dev
    )
    product = jnp.einsum("fip,fjp->fij", cols, cols, precision=lax.Precision.HIGHEST)
    gram_sum = all_sum(product, ("aa", "ba"), n_aa * n_ba)
    upper_factor, inverse = factor(gram_sum)
    pod_modes = math.sqrt(points) * jnp.einsum(
        "fij,fjp->fip", inverse, cols, precision=lax.Precision.HIGHEST
    )
    return (upper_factor, pod_modes)


def solution(mesh):
    placed = (P(("aa", "ba"), None),)
    return jax.shard_map(
        local,
        mesh=mesh,
        in_specs=placed,
        out_specs=(P(), P(None, None, ("aa", "ba"))),
        check_vma=False,
    )
```

```python
import math

import jax
import jax.numpy as jnp
from jax import lax
from jax.experimental import pallas as pl
from jax.experimental.pallas import tpu as pltpu
from jax.sharding import PartitionSpec as P

FREQS = 8


def spectral_rows(block_len, points, first, count):
    sample = first + jnp.arange(count, dtype=jnp.int32)
    harmonic = jnp.arange(1, FREQS + 1, dtype=jnp.int32)
    phase_turns = (sample[:, None] * harmonic[None, :] % block_len).astype(jnp.float32) * (
        2.0 * math.pi / block_len
    )
    full = jnp.arange(block_len, dtype=jnp.int32).astype(jnp.float32) * (2.0 * math.pi / block_len)
    full_window = 0.5 - 0.5 * jnp.cos(full)
    norm_scale = 1.0 / jnp.sqrt(points * jnp.sum(full_window * full_window))
    sample_angle = sample.astype(jnp.float32) * (2.0 * math.pi / block_len)
    window = 0.5 - 0.5 * jnp.cos(sample_angle)
    cosine = window[:, None] * jnp.cos(phase_turns) * norm_scale
    sine = -window[:, None] * jnp.sin(phase_turns) * norm_scale
    return jnp.stack([cosine, sine], axis=1)


def _factor_kernel(a_ref, upper_ref, inv_ref, m_ref):
    freqs, n, _ = a_ref.shape
    rows = lax.broadcasted_iota(jnp.int32, (freqs, n, 2 * n), 1)
    lanes = lax.broadcasted_iota(jnp.int32, (freqs, n, 2 * n), 2)
    m_ref[...] = jnp.concatenate([a_ref[...], (rows[:, :, :n] == lanes[:, :, :n]).astype(jnp.float32)], axis=2)

    def step(j, carry):
        m = m_ref[...]
        pivot_row = m_ref[:, pl.ds(j, 1), :]
        pivot = jnp.sum(jnp.where(lanes[:, :1] == j, pivot_row, 0.0), axis=2, keepdims=True)
        scaled_row = pivot_row / pivot
        column = jnp.sum(jnp.where(lanes == j, m, 0.0), axis=2, keepdims=True)
        column = jnp.where(rows[:, :, :1] > j, column, 0.0)
        m_ref[...] = m - column * scaled_row
        m_ref[:, pl.ds(j, 1), :] = pivot_row / jnp.sqrt(pivot)
        return carry

    lax.fori_loop(0, n, step, 0)
    m = m_ref[...]
    upper_ref[...] = jnp.where(rows[:, :, :n] <= lanes[:, :, :n], m[:, :, :n], 0.0)
    inv_ref[...] = m[:, :, n:]


def factor(gram):
    freqs, n, _ = gram.shape
    return pl.pallas_call(
        _factor_kernel,
        out_shape=(jax.ShapeDtypeStruct(gram.shape, gram.dtype), jax.ShapeDtypeStruct(gram.shape, gram.dtype)),
        scratch_shapes=[pltpu.VMEM((freqs, n, 2 * n), jnp.float32)],
    )(gram)


def all_sum(x, axes, count):
    pieces = x.reshape(count, x.size // count)
    mine = lax.all_to_all(pieces, axes, 0, 0, tiled=True).sum(0, keepdims=True)
    spread = jnp.broadcast_to(mine, pieces.shape)
    return lax.all_to_all(spread, axes, 0, 0, tiled=True).reshape(x.shape)


def local(snapshots):
    time_dev, points = snapshots.shape
    n_aa = lax.axis_size("aa")
    n_ba = lax.axis_size("ba")
    pts_dev = points // (n_aa * n_ba)
    block_len = time_dev * n_ba
    u = lax.axis_index("ba")
    table = spectral_rows(block_len, points, u * time_dev, time_dev)
    arranged = snapshots.reshape(time_dev, n_aa, n_ba, pts_dev)
    partial = jnp.einsum("savq,sgf->vgfaq", arranged, table, precision=lax.Precision.HIGHEST)
    block_spec = lax.all_to_all(partial, "ba", 0, 0, tiled=True).sum(0, keepdims=True)
    spectra = lax.all_to_all(block_spec, "aa", split_axis=3, concat_axis=0, tiled=True)
    blocks = spectra.shape[0]
    columns = 2 * blocks
    cols = jnp.transpose(spectra.reshape(blocks, 2, FREQS, pts_dev), (2, 0, 1, 3)).reshape(
        FREQS, columns, pts_dev
    )
    product = jnp.einsum("fip,fjp->fij", cols, cols, precision=lax.Precision.HIGHEST)
    gram_sum = all_sum(product, ("aa", "ba"), n_aa * n_ba)
    upper_factor, inverse = factor(gram_sum)
    pod_modes = math.sqrt(points) * jnp.einsum(
        "fij,fjp->fip", inverse, cols, precision=lax.Precision.HIGHEST
    )
    return (upper_factor, pod_modes)


def solution(mesh):
    placed = (P(("aa", "ba"), None),)
    return jax.shard_map(
        local,
        mesh=mesh,
        in_specs=placed,
        out_specs=(P(), P(None, None, ("aa", "ba"))),
        check_vma=False,
    )
```

```python
import math

import jax
import jax.numpy as jnp
from jax import lax
from jax.experimental import pallas as pl
from jax.experimental.pallas import tpu as pltpu
from jax.sharding import PartitionSpec as P

FREQS = 8


def spectral_rows(block_len, points, first, count):
    sample = first + jnp.arange(count, dtype=jnp.int32)
    harmonic = jnp.arange(1, FREQS + 1, dtype=jnp.int32)
    phase_turns = (sample[:, None] * harmonic[None, :] % block_len).astype(jnp.float32) * (
        2.0 * math.pi / block_len
    )
    full = jnp.arange(block_len, dtype=jnp.int32).astype(jnp.float32) * (2.0 * math.pi / block_len)
    full_window = 0.5 - 0.5 * jnp.cos(full)
    norm_scale = 1.0 / jnp.sqrt(points * jnp.sum(full_window * full_window))
    sample_angle = sample.astype(jnp.float32) * (2.0 * math.pi / block_len)
    window = 0.5 - 0.5 * jnp.cos(sample_angle)
    cosine = window[:, None] * jnp.cos(phase_turns) * norm_scale
    sine = -window[:, None] * jnp.sin(phase_turns) * norm_scale
    return jnp.stack([cosine, sine], axis=1)


def _factor_kernel(a_ref, upper_ref, inv_ref, m_ref):
    freqs, n, _ = a_ref.shape
    rows = lax.broadcasted_iota(jnp.int32, (freqs, n, 2 * n), 1)
    lanes = lax.broadcasted_iota(jnp.int32, (freqs, n, 2 * n), 2)
    m_ref[...] = jnp.concatenate([a_ref[...], (rows[:, :, :n] == lanes[:, :, :n]).astype(jnp.float32)], axis=2)

    def step(j, carry):
        m = m_ref[...]
        pivot_row = m_ref[:, pl.ds(j, 1), :]
        pivot = jnp.sum(jnp.where(lanes[:, :1] == j, pivot_row, 0.0), axis=2, keepdims=True)
        scaled_row = pivot_row / pivot
        column = jnp.sum(jnp.where(lanes == j, m, 0.0), axis=2, keepdims=True)
        column = jnp.where(rows[:, :, :1] > j, column, 0.0)
        m_ref[...] = m - column * scaled_row
        m_ref[:, pl.ds(j, 1), :] = pivot_row / jnp.sqrt(pivot)
        return carry

    lax.fori_loop(0, n, step, 0)
    m = m_ref[...]
    upper_ref[...] = jnp.where(rows[:, :, :n] <= lanes[:, :, :n], m[:, :, :n], 0.0)
    inv_ref[...] = m[:, :, n:]


def factor(gram):
    freqs, n, _ = gram.shape
    return pl.pallas_call(
        _factor_kernel,
        out_shape=(jax.ShapeDtypeStruct(gram.shape, gram.dtype), jax.ShapeDtypeStruct(gram.shape, gram.dtype)),
        scratch_shapes=[pltpu.VMEM((freqs, n, 2 * n), jnp.float32)],
    )(gram)


def all_sum(x, axes, count):
    pieces = x.reshape(count, x.size // count)
    mine = lax.all_to_all(pieces, axes, 0, 0, tiled=True).sum(0, keepdims=True)
    spread = jnp.broadcast_to(mine, pieces.shape)
    return lax.all_to_all(spread, axes, 0, 0, tiled=True).reshape(x.shape)


def sum_over_ba(partial, n_ba):
    u = lax.axis_index("ba")
    cores = 2
    if n_ba % cores:
        return lax.all_to_all(partial, "ba", 0, 0, tiled=True).sum(0, keepdims=True)
    chips = n_ba // cores
    y, c = u // cores, u % cores
    parts = partial.reshape(chips, cores, *partial.shape[1:])
    send = lax.dynamic_index_in_dim(parts, cores - 1 - c, axis=1, keepdims=False)
    keep = lax.dynamic_index_in_dim(parts, c, axis=1, keepdims=False)
    chip_sum = keep + lax.ppermute(send, "ba", [(i, i ^ 1) for i in range(n_ba)])
    total = lax.dynamic_index_in_dim(chip_sum, y, axis=0, keepdims=True)
    for shift in range(1, chips):
        out = lax.dynamic_index_in_dim(chip_sum, (y + shift) % chips, axis=0, keepdims=True)
        perm = [(i, ((i // cores + shift) % chips) * cores + i % cores) for i in range(n_ba)]
        total = total + lax.ppermute(out, "ba", perm)
    return total


def local(snapshots):
    time_dev, points = snapshots.shape
    n_aa = lax.axis_size("aa")
    n_ba = lax.axis_size("ba")
    pts_dev = points // (n_aa * n_ba)
    block_len = time_dev * n_ba
    u = lax.axis_index("ba")
    table = spectral_rows(block_len, points, u * time_dev, time_dev)
    arranged = snapshots.reshape(time_dev, n_aa, n_ba, pts_dev)
    partial = jnp.einsum("savq,sgf->vgfaq", arranged, table, precision=lax.Precision.HIGHEST)
    block_spec = sum_over_ba(partial, n_ba)
    spectra = lax.all_to_all(block_spec, "aa", split_axis=3, concat_axis=0, tiled=True)
    blocks = spectra.shape[0]
    columns = 2 * blocks
    cols = jnp.transpose(spectra.reshape(blocks, 2, FREQS, pts_dev), (2, 0, 1, 3)).reshape(
        FREQS, columns, pts_dev
    )
    product = jnp.einsum("fip,fjp->fij", cols, cols, precision=lax.Precision.HIGHEST)
    gram_sum = all_sum(product, ("aa", "ba"), n_aa * n_ba)
    upper_factor, inverse = factor(gram_sum)
    pod_modes = math.sqrt(points) * jnp.einsum(
        "fij,fjp->fip", inverse, cols, precision=lax.Precision.HIGHEST
    )
    return (upper_factor, pod_modes)


def solution(mesh):
    placed = (P(("aa", "ba"), None),)
    return jax.shard_map(
        local,
        mesh=mesh,
        in_specs=placed,
        out_specs=(P(), P(None, None, ("aa", "ba"))),
        check_vma=False,
    )
```

```python
import math

import jax
import jax.numpy as jnp
from jax import lax
from jax.experimental import pallas as pl
from jax.experimental.pallas import tpu as pltpu
from jax.sharding import PartitionSpec as P

FREQS = 8


def spectral_rows(block_len, points, first, count):
    sample = first + jnp.arange(count, dtype=jnp.int32)
    harmonic = jnp.arange(1, FREQS + 1, dtype=jnp.int32)
    phase_turns = (sample[:, None] * harmonic[None, :] % block_len).astype(jnp.float32) * (
        2.0 * math.pi / block_len
    )
    full = jnp.arange(block_len, dtype=jnp.int32).astype(jnp.float32) * (2.0 * math.pi / block_len)
    full_window = 0.5 - 0.5 * jnp.cos(full)
    norm_scale = 1.0 / jnp.sqrt(points * jnp.sum(full_window * full_window))
    sample_angle = sample.astype(jnp.float32) * (2.0 * math.pi / block_len)
    window = 0.5 - 0.5 * jnp.cos(sample_angle)
    cosine = window[:, None] * jnp.cos(phase_turns) * norm_scale
    sine = -window[:, None] * jnp.sin(phase_turns) * norm_scale
    return jnp.stack([cosine, sine], axis=1)


def _factor_kernel(a_ref, upper_ref, inv_ref, m_ref):
    freqs, n, _ = a_ref.shape
    rows = lax.broadcasted_iota(jnp.int32, (freqs, n, 2 * n), 1)
    lanes = lax.broadcasted_iota(jnp.int32, (freqs, n, 2 * n), 2)
    m_ref[...] = jnp.concatenate([a_ref[...], (rows[:, :, :n] == lanes[:, :, :n]).astype(jnp.float32)], axis=2)

    def step(j, carry):
        m = m_ref[...]
        pivot_row = m_ref[:, pl.ds(j, 1), :]
        pivot = jnp.sum(jnp.where(lanes[:, :1] == j, pivot_row, 0.0), axis=2, keepdims=True)
        scaled_row = pivot_row / pivot
        column = jnp.sum(jnp.where(lanes == j, m, 0.0), axis=2, keepdims=True)
        column = jnp.where(rows[:, :, :1] > j, column, 0.0)
        m_ref[...] = m - column * scaled_row
        m_ref[:, pl.ds(j, 1), :] = pivot_row / jnp.sqrt(pivot)
        return carry

    lax.fori_loop(0, n, step, 0)
    m = m_ref[...]
    upper_ref[...] = jnp.where(rows[:, :, :n] <= lanes[:, :, :n], m[:, :, :n], 0.0)
    inv_ref[...] = m[:, :, n:]


def factor(gram):
    freqs, n, _ = gram.shape
    return pl.pallas_call(
        _factor_kernel,
        out_shape=(jax.ShapeDtypeStruct(gram.shape, gram.dtype), jax.ShapeDtypeStruct(gram.shape, gram.dtype)),
        scratch_shapes=[pltpu.VMEM((freqs, n, 2 * n), jnp.float32)],
    )(gram)


def all_sum(x, axes, count):
    pieces = x.reshape(count, x.size // count)
    mine = lax.all_to_all(pieces, axes, 0, 0, tiled=True).sum(0, keepdims=True)
    spread = jnp.broadcast_to(mine, pieces.shape)
    return lax.all_to_all(spread, axes, 0, 0, tiled=True).reshape(x.shape)


def _dft_kernel(table_ref, snap_ref, out_ref):
    n_ba, a_step, _, pts_dev = out_ref.shape
    res = jnp.dot(table_ref[...], snap_ref[...], precision=lax.Precision.HIGHEST,
                  preferred_element_type=jnp.float32)
    for a in range(a_step):
        for v in range(n_ba):
            start = (a * n_ba + v) * pts_dev
            out_ref[v, a] = res[:, start:start + pts_dev]


def partial_dft(table_t, snapshots, n_aa, n_ba):
    a_step = math.gcd(4, n_aa)
    rows, time_dev = table_t.shape
    points = snapshots.shape[1]
    pts_dev = points // (n_aa * n_ba)
    width = a_step * n_ba * pts_dev
    return pl.pallas_call(
        _dft_kernel,
        grid=(n_aa // a_step,),
        in_specs=[
            pl.BlockSpec((rows, time_dev), lambda i: (0, 0)),
            pl.BlockSpec((time_dev, width), lambda i: (0, i)),
        ],
        out_specs=pl.BlockSpec((n_ba, a_step, rows, pts_dev), lambda i: (0, i, 0, 0)),
        out_shape=jax.ShapeDtypeStruct((n_ba, n_aa, rows, pts_dev), jnp.float32),
    )(table_t, snapshots)


def sum_over_ba(partial, n_ba):
    u = lax.axis_index("ba")
    cores = 2
    if n_ba % cores:
        return lax.all_to_all(partial, "ba", 0, 0, tiled=True).sum(0, keepdims=True)
    chips = n_ba // cores
    y, c = u // cores, u % cores
    parts = partial.reshape(chips, cores, *partial.shape[1:])
    send = lax.dynamic_index_in_dim(parts, cores - 1 - c, axis=1, keepdims=False)
    keep = lax.dynamic_index_in_dim(parts, c, axis=1, keepdims=False)
    chip_sum = keep + lax.ppermute(send, "ba", [(i, i ^ 1) for i in range(n_ba)])
    total = lax.dynamic_index_in_dim(chip_sum, y, axis=0, keepdims=True)
    for shift in range(1, chips):
        out = lax.dynamic_index_in_dim(chip_sum, (y + shift) % chips, axis=0, keepdims=True)
        perm = [(i, ((i // cores + shift) % chips) * cores + i % cores) for i in range(n_ba)]
        total = total + lax.ppermute(out, "ba", perm)
    return total


def local(snapshots):
    time_dev, points = snapshots.shape
    n_aa = lax.axis_size("aa")
    n_ba = lax.axis_size("ba")
    pts_dev = points // (n_aa * n_ba)
    block_len = time_dev * n_ba
    u = lax.axis_index("ba")
    table = spectral_rows(block_len, points, u * time_dev, time_dev)
    table_t = jnp.transpose(table, (2, 1, 0)).reshape(2 * FREQS, time_dev)
    partial = partial_dft(table_t, snapshots, n_aa, n_ba)
    block_spec = sum_over_ba(partial, n_ba)
    spectra = lax.all_to_all(block_spec, "aa", split_axis=1, concat_axis=0, tiled=True)
    blocks = spectra.shape[0]
    columns = 2 * blocks
    cols = jnp.transpose(spectra.reshape(blocks, FREQS, 2, pts_dev), (1, 0, 2, 3)).reshape(
        FREQS, columns, pts_dev
    )
    product = jnp.einsum("fip,fjp->fij", cols, cols, precision=lax.Precision.HIGHEST)
    gram_sum = all_sum(product, ("aa", "ba"), n_aa * n_ba)
    upper_factor, inverse = factor(gram_sum)
    pod_modes = math.sqrt(points) * jnp.einsum(
        "fij,fjp->fip", inverse, cols, precision=lax.Precision.HIGHEST
    )
    return (upper_factor, pod_modes)


def solution(mesh):
    placed = (P(("aa", "ba"), None),)
    return jax.shard_map(
        local,
        mesh=mesh,
        in_specs=placed,
        out_specs=(P(), P(None, None, ("aa", "ba"))),
        check_vma=False,
    )
```

```python
import math

import jax
import jax.numpy as jnp
from jax import lax
from jax.experimental import pallas as pl
from jax.experimental.pallas import tpu as pltpu
from jax.sharding import PartitionSpec as P

FREQS = 8


def spectral_rows(block_len, points, first, count):
    sample = first + jnp.arange(count, dtype=jnp.int32)
    harmonic = jnp.arange(1, FREQS + 1, dtype=jnp.int32)
    phase_turns = (sample[:, None] * harmonic[None, :] % block_len).astype(jnp.float32) * (
        2.0 * math.pi / block_len
    )
    full = jnp.arange(block_len, dtype=jnp.int32).astype(jnp.float32) * (2.0 * math.pi / block_len)
    full_window = 0.5 - 0.5 * jnp.cos(full)
    norm_scale = 1.0 / jnp.sqrt(points * jnp.sum(full_window * full_window))
    sample_angle = sample.astype(jnp.float32) * (2.0 * math.pi / block_len)
    window = 0.5 - 0.5 * jnp.cos(sample_angle)
    cosine = window[:, None] * jnp.cos(phase_turns) * norm_scale
    sine = -window[:, None] * jnp.sin(phase_turns) * norm_scale
    return jnp.stack([cosine, sine], axis=1)


def _factor_kernel(a_ref, upper_ref, inv_ref, m_ref):
    freqs, n, _ = a_ref.shape
    rows = lax.broadcasted_iota(jnp.int32, (freqs, n, 2 * n), 1)
    lanes = lax.broadcasted_iota(jnp.int32, (freqs, n, 2 * n), 2)
    m_ref[...] = jnp.concatenate([a_ref[...], (rows[:, :, :n] == lanes[:, :, :n]).astype(jnp.float32)], axis=2)

    def step(j, carry):
        m = m_ref[...]
        pivot_row = m_ref[:, pl.ds(j, 1), :]
        pivot = jnp.sum(jnp.where(lanes[:, :1] == j, pivot_row, 0.0), axis=2, keepdims=True)
        scaled_row = pivot_row / pivot
        column = jnp.sum(jnp.where(lanes == j, m, 0.0), axis=2, keepdims=True)
        column = jnp.where(rows[:, :, :1] > j, column, 0.0)
        m_ref[...] = m - column * scaled_row
        m_ref[:, pl.ds(j, 1), :] = pivot_row / jnp.sqrt(pivot)
        return carry

    lax.fori_loop(0, n, step, 0)
    m = m_ref[...]
    upper_ref[...] = jnp.where(rows[:, :, :n] <= lanes[:, :, :n], m[:, :, :n], 0.0)
    inv_ref[...] = m[:, :, n:]


def factor(gram):
    freqs, n, _ = gram.shape
    return pl.pallas_call(
        _factor_kernel,
        out_shape=(jax.ShapeDtypeStruct(gram.shape, gram.dtype), jax.ShapeDtypeStruct(gram.shape, gram.dtype)),
        scratch_shapes=[pltpu.VMEM((freqs, n, 2 * n), jnp.float32)],
    )(gram)


def all_sum(x, axes, count):
    pieces = x.reshape(count, x.size // count)
    mine = lax.all_to_all(pieces, axes, 0, 0, tiled=True).sum(0, keepdims=True)
    spread = jnp.broadcast_to(mine, pieces.shape)
    return lax.all_to_all(spread, axes, 0, 0, tiled=True).reshape(x.shape)


def _dft_kernel(table_ref, snap_ref, out_ref):
    halves, n_ba, a_step, rows, pts_dev = out_ref.shape
    res = jnp.dot(table_ref[...], snap_ref[...], precision=lax.Precision.HIGHEST,
                  preferred_element_type=jnp.float32)
    for h in range(halves):
        for a in range(a_step):
            for v in range(n_ba):
                start = (a * n_ba + v) * pts_dev
                out_ref[h, v, a] = res[h * rows:(h + 1) * rows, start:start + pts_dev]


def partial_dft(table_t, snapshots, n_aa, n_ba, halves):
    a_step = math.gcd(4, n_aa)
    rows, time_dev = table_t.shape
    points = snapshots.shape[1]
    pts_dev = points // (n_aa * n_ba)
    width = a_step * n_ba * pts_dev
    return pl.pallas_call(
        _dft_kernel,
        grid=(n_aa // a_step,),
        in_specs=[
            pl.BlockSpec((rows, time_dev), lambda i: (0, 0)),
            pl.BlockSpec((time_dev, width), lambda i: (0, i)),
        ],
        out_specs=pl.BlockSpec((halves, n_ba, a_step, rows // halves, pts_dev), lambda i: (0, 0, i, 0, 0)),
        out_shape=jax.ShapeDtypeStruct((halves, n_ba, n_aa, rows // halves, pts_dev), jnp.float32),
    )(table_t, snapshots)


def sum_over_ba(partial, n_ba):
    u = lax.axis_index("ba")
    cores = 2
    if n_ba % cores:
        return lax.all_to_all(partial, "ba", 0, 0, tiled=True).sum(0, keepdims=True)
    chips = n_ba // cores
    y, c = u // cores, u % cores
    parts = partial.reshape(chips, cores, *partial.shape[1:])
    send = lax.dynamic_index_in_dim(parts, cores - 1 - c, axis=1, keepdims=False)
    keep = lax.dynamic_index_in_dim(parts, c, axis=1, keepdims=False)
    chip_sum = keep + lax.ppermute(send, "ba", [(i, i ^ 1) for i in range(n_ba)])
    total = lax.dynamic_index_in_dim(chip_sum, y, axis=0, keepdims=True)
    for shift in range(1, chips):
        out = lax.dynamic_index_in_dim(chip_sum, (y + shift) % chips, axis=0, keepdims=True)
        perm = [(i, ((i // cores + shift) % chips) * cores + i % cores) for i in range(n_ba)]
        total = total + lax.ppermute(out, "ba", perm)
    return total


def local(snapshots):
    time_dev, points = snapshots.shape
    n_aa = lax.axis_size("aa")
    n_ba = lax.axis_size("ba")
    pts_dev = points // (n_aa * n_ba)
    block_len = time_dev * n_ba
    u = lax.axis_index("ba")
    table = spectral_rows(block_len, points, u * time_dev, time_dev)
    table_t = jnp.transpose(table, (2, 1, 0)).reshape(2 * FREQS, time_dev)
    halves = 2
    partial = partial_dft(table_t, snapshots, n_aa, n_ba, halves)
    shares = []
    for h in range(halves):
        block_spec = sum_over_ba(partial[h], n_ba)
        shares.append(lax.all_to_all(block_spec, "aa", split_axis=1, concat_axis=0, tiled=True))
    spectra = jnp.concatenate(shares, axis=2)
    blocks = spectra.shape[0]
    columns = 2 * blocks
    cols = jnp.transpose(spectra.reshape(blocks, FREQS, 2, pts_dev), (1, 0, 2, 3)).reshape(
        FREQS, columns, pts_dev
    )
    product = jnp.einsum("fip,fjp->fij", cols, cols, precision=lax.Precision.HIGHEST)
    gram_sum = all_sum(product, ("aa", "ba"), n_aa * n_ba)
    upper_factor, inverse = factor(gram_sum)
    pod_modes = math.sqrt(points) * jnp.einsum(
        "fij,fjp->fip", inverse, cols, precision=lax.Precision.HIGHEST
    )
    return (upper_factor, pod_modes)


def solution(mesh):
    placed = (P(("aa", "ba"), None),)
    return jax.shard_map(
        local,
        mesh=mesh,
        in_specs=placed,
        out_specs=(P(), P(None, None, ("aa", "ba"))),
        check_vma=False,
    )
```

```python
import math

import jax
import jax.numpy as jnp
from jax import lax
from jax.experimental import pallas as pl
from jax.experimental.pallas import tpu as pltpu
from jax.sharding import PartitionSpec as P

FREQS = 8


def spectral_rows(block_len, points, first, count):
    sample = first + jnp.arange(count, dtype=jnp.int32)
    harmonic = jnp.arange(1, FREQS + 1, dtype=jnp.int32)
    phase_turns = (sample[:, None] * harmonic[None, :] % block_len).astype(jnp.float32) * (
        2.0 * math.pi / block_len
    )
    full = jnp.arange(block_len, dtype=jnp.int32).astype(jnp.float32) * (2.0 * math.pi / block_len)
    full_window = 0.5 - 0.5 * jnp.cos(full)
    norm_scale = 1.0 / jnp.sqrt(points * jnp.sum(full_window * full_window))
    sample_angle = sample.astype(jnp.float32) * (2.0 * math.pi / block_len)
    window = 0.5 - 0.5 * jnp.cos(sample_angle)
    cosine = window[:, None] * jnp.cos(phase_turns) * norm_scale
    sine = -window[:, None] * jnp.sin(phase_turns) * norm_scale
    return jnp.stack([cosine, sine], axis=1)


def _factor_kernel(a_ref, upper_ref, inv_ref, m_ref):
    freqs, n, _ = a_ref.shape
    rows = lax.broadcasted_iota(jnp.int32, (freqs, n, 2 * n), 1)
    lanes = lax.broadcasted_iota(jnp.int32, (freqs, n, 2 * n), 2)
    m_ref[...] = jnp.concatenate([a_ref[...], (rows[:, :, :n] == lanes[:, :, :n]).astype(jnp.float32)], axis=2)
    tile = math.gcd(8, n)
    for lo in range(0, n, tile):
        def step(jj, carry, lo=lo):
            j = lo + jj
            m = m_ref[:, lo:, :]
            pivot_row = m_ref[:, pl.ds(j, 1), :]
            pivot = jnp.sum(jnp.where(lanes[:, :1] == j, pivot_row, 0.0), axis=2, keepdims=True)
            scaled_row = pivot_row / pivot
            column = jnp.sum(jnp.where(lanes[:, lo:] == j, m, 0.0), axis=2, keepdims=True)
            column = jnp.where(rows[:, lo:, :1] > j, column, 0.0)
            m_ref[:, lo:, :] = m - column * scaled_row
            m_ref[:, pl.ds(j, 1), :] = pivot_row / jnp.sqrt(pivot)
            return carry

        lax.fori_loop(0, tile, step, 0)
    m = m_ref[...]
    upper_ref[...] = jnp.where(rows[:, :, :n] <= lanes[:, :, :n], m[:, :, :n], 0.0)
    inv_ref[...] = m[:, :, n:]


def factor(gram):
    freqs, n, _ = gram.shape
    return pl.pallas_call(
        _factor_kernel,
        out_shape=(jax.ShapeDtypeStruct(gram.shape, gram.dtype), jax.ShapeDtypeStruct(gram.shape, gram.dtype)),
        scratch_shapes=[pltpu.VMEM((freqs, n, 2 * n), jnp.float32)],
    )(gram)


def all_sum(x, axes, count):
    pieces = x.reshape(count, x.size // count)
    mine = lax.all_to_all(pieces, axes, 0, 0, tiled=True).sum(0, keepdims=True)
    spread = jnp.broadcast_to(mine, pieces.shape)
    return lax.all_to_all(spread, axes, 0, 0, tiled=True).reshape(x.shape)


def _dft_kernel(table_ref, snap_ref, out_ref):
    n_ba, a_step, _, pts_dev = out_ref.shape
    res = jnp.dot(table_ref[...], snap_ref[...], precision=lax.Precision.HIGHEST,
                  preferred_element_type=jnp.float32)
    for a in range(a_step):
        for v in range(n_ba):
            start = (a * n_ba + v) * pts_dev
            out_ref[v, a] = res[:, start:start + pts_dev]


def partial_dft(table_t, snapshots, n_aa, n_ba):
    a_step = math.gcd(4, n_aa)
    rows, time_dev = table_t.shape
    points = snapshots.shape[1]
    pts_dev = points // (n_aa * n_ba)
    width = a_step * n_ba * pts_dev
    return pl.pallas_call(
        _dft_kernel,
        grid=(n_aa // a_step,),
        in_specs=[
            pl.BlockSpec((rows, time_dev), lambda i: (0, 0)),
            pl.BlockSpec((time_dev, width), lambda i: (0, i)),
        ],
        out_specs=pl.BlockSpec((n_ba, a_step, rows, pts_dev), lambda i: (0, i, 0, 0)),
        out_shape=jax.ShapeDtypeStruct((n_ba, n_aa, rows, pts_dev), jnp.float32),
    )(table_t, snapshots)


def sum_over_ba(partial, n_ba):
    u = lax.axis_index("ba")
    cores = 2
    if n_ba % cores:
        return lax.all_to_all(partial, "ba", 0, 0, tiled=True).sum(0, keepdims=True)
    chips = n_ba // cores
    y, c = u // cores, u % cores
    parts = partial.reshape(chips, cores, *partial.shape[1:])
    send = lax.dynamic_index_in_dim(parts, cores - 1 - c, axis=1, keepdims=False)
    keep = lax.dynamic_index_in_dim(parts, c, axis=1, keepdims=False)
    chip_sum = keep + lax.ppermute(send, "ba", [(i, i ^ 1) for i in range(n_ba)])
    total = lax.dynamic_index_in_dim(chip_sum, y, axis=0, keepdims=True)
    for shift in range(1, chips):
        out = lax.dynamic_index_in_dim(chip_sum, (y + shift) % chips, axis=0, keepdims=True)
        perm = [(i, ((i // cores + shift) % chips) * cores + i % cores) for i in range(n_ba)]
        total = total + lax.ppermute(out, "ba", perm)
    return total


def local(snapshots):
    time_dev, points = snapshots.shape
    n_aa = lax.axis_size("aa")
    n_ba = lax.axis_size("ba")
    pts_dev = points // (n_aa * n_ba)
    block_len = time_dev * n_ba
    u = lax.axis_index("ba")
    table = spectral_rows(block_len, points, u * time_dev, time_dev)
    table_t = jnp.transpose(table, (2, 1, 0)).reshape(2 * FREQS, time_dev)
    partial = partial_dft(table_t, snapshots, n_aa, n_ba)
    block_spec = sum_over_ba(partial, n_ba)
    spectra = lax.all_to_all(block_spec, "aa", split_axis=1, concat_axis=0, tiled=True)
    blocks = spectra.shape[0]
    columns = 2 * blocks
    cols = jnp.transpose(spectra.reshape(blocks, FREQS, 2, pts_dev), (1, 0, 2, 3)).reshape(
        FREQS, columns, pts_dev
    )
    product = jnp.einsum("fip,fjp->fij", cols, cols, precision=lax.Precision.HIGHEST)
    gram_sum = all_sum(product, ("aa", "ba"), n_aa * n_ba)
    upper_factor, inverse = factor(gram_sum)
    pod_modes = math.sqrt(points) * jnp.einsum(
        "fij,fjp->fip", inverse, cols, precision=lax.Precision.HIGHEST
    )
    return (upper_factor, pod_modes)


def solution(mesh):
    placed = (P(("aa", "ba"), None),)
    return jax.shard_map(
        local,
        mesh=mesh,
        in_specs=placed,
        out_specs=(P(), P(None, None, ("aa", "ba"))),
        check_vma=False,
    )
```

```python
import math

import jax
import jax.numpy as jnp
from jax import lax
from jax.experimental import pallas as pl
from jax.experimental.pallas import tpu as pltpu
from jax.sharding import PartitionSpec as P

FREQS = 8


def spectral_rows(block_len, points, first, count):
    sample = first + jnp.arange(count, dtype=jnp.int32)
    harmonic = jnp.arange(1, FREQS + 1, dtype=jnp.int32)
    phase_turns = (sample[:, None] * harmonic[None, :] % block_len).astype(jnp.float32) * (
        2.0 * math.pi / block_len
    )
    full = jnp.arange(block_len, dtype=jnp.int32).astype(jnp.float32) * (2.0 * math.pi / block_len)
    full_window = 0.5 - 0.5 * jnp.cos(full)
    norm_scale = 1.0 / jnp.sqrt(points * jnp.sum(full_window * full_window))
    sample_angle = sample.astype(jnp.float32) * (2.0 * math.pi / block_len)
    window = 0.5 - 0.5 * jnp.cos(sample_angle)
    cosine = window[:, None] * jnp.cos(phase_turns) * norm_scale
    sine = -window[:, None] * jnp.sin(phase_turns) * norm_scale
    return jnp.stack([cosine, sine], axis=1)


def _factor_kernel(a_ref, upper_ref, inv_ref, m_ref):
    freqs, n, _ = a_ref.shape
    rows = lax.broadcasted_iota(jnp.int32, (freqs, n, 2 * n), 1)
    lanes = lax.broadcasted_iota(jnp.int32, (freqs, n, 2 * n), 2)
    m_ref[...] = jnp.concatenate([a_ref[...], (rows[:, :, :n] == lanes[:, :, :n]).astype(jnp.float32)], axis=2)
    tile = math.gcd(8, n)
    for lo in range(0, n, tile):
        def step(jj, carry, lo=lo):
            j = lo + jj
            m = m_ref[:, lo:, :]
            pivot_row = m_ref[:, pl.ds(j, 1), :]
            pivot = jnp.sum(jnp.where(lanes[:, :1] == j, pivot_row, 0.0), axis=2, keepdims=True)
            scaled_row = pivot_row / pivot
            column = jnp.sum(jnp.where(lanes[:, lo:] == j, m, 0.0), axis=2, keepdims=True)
            column = jnp.where(rows[:, lo:, :1] > j, column, 0.0)
            m_ref[:, lo:, :] = m - column * scaled_row
            m_ref[:, pl.ds(j, 1), :] = pivot_row / jnp.sqrt(pivot)
            return carry

        lax.fori_loop(0, tile, step, 0)
    m = m_ref[...]
    upper_ref[...] = jnp.where(rows[:, :, :n] <= lanes[:, :, :n], m[:, :, :n], 0.0)
    inv_ref[...] = m[:, :, n:]


def factor(gram):
    freqs, n, _ = gram.shape
    return pl.pallas_call(
        _factor_kernel,
        out_shape=(jax.ShapeDtypeStruct(gram.shape, gram.dtype), jax.ShapeDtypeStruct(gram.shape, gram.dtype)),
        scratch_shapes=[pltpu.VMEM((freqs, n, 2 * n), jnp.float32)],
    )(gram)


def all_sum(x, axes, count):
    pieces = x.reshape(count, x.size // count)
    mine = lax.all_to_all(pieces, axes, 0, 0, tiled=True).sum(0, keepdims=True)
    spread = jnp.broadcast_to(mine, pieces.shape)
    return lax.all_to_all(spread, axes, 0, 0, tiled=True).reshape(x.shape)


def _dft_kernel(core_ref, table_ref, snap_ref, out_ref):
    _, chips, a_step, _, pts_dev = out_ref.shape
    core = core_ref[0]
    res = jnp.dot(table_ref[...], snap_ref[...], precision=lax.Precision.HIGHEST,
                  preferred_element_type=jnp.float32)
    for a in range(a_step):
        for v in range(2 * chips):
            cv = v % 2
            keep = 1 - (cv + core - 2 * cv * core)
            start = (a * 2 * chips + v) * pts_dev
            out_ref[keep, v // 2, a] = res[:, start:start + pts_dev]


def partial_dft(table_t, snapshots, core, n_aa, n_ba):
    a_step = math.gcd(4, n_aa)
    rows, time_dev = table_t.shape
    points = snapshots.shape[1]
    pts_dev = points // (n_aa * n_ba)
    width = a_step * n_ba * pts_dev
    return pl.pallas_call(
        _dft_kernel,
        grid_spec=pltpu.PrefetchScalarGridSpec(
            num_scalar_prefetch=1,
            grid=(n_aa // a_step,),
            in_specs=[
                pl.BlockSpec((rows, time_dev), lambda i, c: (0, 0)),
                pl.BlockSpec((time_dev, width), lambda i, c: (0, i)),
            ],
            out_specs=pl.BlockSpec((2, n_ba // 2, a_step, rows, pts_dev), lambda i, c: (0, 0, i, 0, 0)),
        ),
        out_shape=jax.ShapeDtypeStruct((2, n_ba // 2, n_aa, rows, pts_dev), jnp.float32),
    )(core, table_t, snapshots)


def sum_over_ba(partial, n_ba):
    u = lax.axis_index("ba")
    cores = 2
    chips = n_ba // cores
    y = u // cores
    chip_sum = partial[1] + lax.ppermute(partial[0], "ba", [(i, i ^ 1) for i in range(n_ba)])
    total = lax.dynamic_index_in_dim(chip_sum, y, axis=0, keepdims=True)
    for shift in range(1, chips):
        out = lax.dynamic_index_in_dim(chip_sum, (y + shift) % chips, axis=0, keepdims=True)
        perm = [(i, ((i // cores + shift) % chips) * cores + i % cores) for i in range(n_ba)]
        total = total + lax.ppermute(out, "ba", perm)
    return total


def local(snapshots):
    time_dev, points = snapshots.shape
    n_aa = lax.axis_size("aa")
    n_ba = lax.axis_size("ba")
    pts_dev = points // (n_aa * n_ba)
    block_len = time_dev * n_ba
    u = lax.axis_index("ba")
    table = spectral_rows(block_len, points, u * time_dev, time_dev)
    table_t = jnp.transpose(table, (2, 1, 0)).reshape(2 * FREQS, time_dev)
    core = (u % 2).astype(jnp.int32).reshape(1)
    partial = partial_dft(table_t, snapshots, core, n_aa, n_ba)
    block_spec = sum_over_ba(partial, n_ba)
    spectra = lax.all_to_all(block_spec, "aa", split_axis=1, concat_axis=0, tiled=True)
    blocks = spectra.shape[0]
    columns = 2 * blocks
    cols = jnp.transpose(spectra.reshape(blocks, FREQS, 2, pts_dev), (1, 0, 2, 3)).reshape(
        FREQS, columns, pts_dev
    )
    product = jnp.einsum("fip,fjp->fij", cols, cols, precision=lax.Precision.HIGHEST)
    gram_sum = all_sum(product, ("aa", "ba"), n_aa * n_ba)
    upper_factor, inverse = factor(gram_sum)
    pod_modes = math.sqrt(points) * jnp.einsum(
        "fij,fjp->fip", inverse, cols, precision=lax.Precision.HIGHEST
    )
    return (upper_factor, pod_modes)


def solution(mesh):
    placed = (P(("aa", "ba"), None),)
    return jax.shard_map(
        local,
        mesh=mesh,
        in_specs=placed,
        out_specs=(P(), P(None, None, ("aa", "ba"))),
        check_vma=False,
    )
```

```python
import math

import jax
import jax.numpy as jnp
from jax import lax
from jax.experimental import pallas as pl
from jax.experimental.pallas import tpu as pltpu
from jax.sharding import PartitionSpec as P

FREQS = 8


def spectral_rows(block_len, points, first, count):
    sample = first + jnp.arange(count, dtype=jnp.int32)
    harmonic = jnp.arange(1, FREQS + 1, dtype=jnp.int32)
    phase_turns = (sample[:, None] * harmonic[None, :] % block_len).astype(jnp.float32) * (
        2.0 * math.pi / block_len
    )
    full = jnp.arange(block_len, dtype=jnp.int32).astype(jnp.float32) * (2.0 * math.pi / block_len)
    full_window = 0.5 - 0.5 * jnp.cos(full)
    norm_scale = 1.0 / jnp.sqrt(points * jnp.sum(full_window * full_window))
    sample_angle = sample.astype(jnp.float32) * (2.0 * math.pi / block_len)
    window = 0.5 - 0.5 * jnp.cos(sample_angle)
    cosine = window[:, None] * jnp.cos(phase_turns) * norm_scale
    sine = -window[:, None] * jnp.sin(phase_turns) * norm_scale
    return jnp.stack([cosine, sine], axis=1)


def _factor_kernel(a_ref, upper_ref, inv_ref, m_ref):
    freqs, n, _ = a_ref.shape
    rows = lax.broadcasted_iota(jnp.int32, (freqs, n, 2 * n), 1)
    lanes = lax.broadcasted_iota(jnp.int32, (freqs, n, 2 * n), 2)
    m_ref[...] = jnp.concatenate([a_ref[...], (rows[:, :, :n] == lanes[:, :, :n]).astype(jnp.float32)], axis=2)
    tile = math.gcd(8, n)
    for lo in range(0, n, tile):
        def step(jj, carry, lo=lo):
            j = lo + jj
            m = m_ref[:, lo:, :]
            pivot_row = m_ref[:, pl.ds(j, 1), :]
            pivot = jnp.sum(jnp.where(lanes[:, :1] == j, pivot_row, 0.0), axis=2, keepdims=True)
            scaled_row = pivot_row / pivot
            column = jnp.sum(jnp.where(lanes[:, lo:] == j, m, 0.0), axis=2, keepdims=True)
            column = jnp.where(rows[:, lo:, :1] > j, column, 0.0)
            m_ref[:, lo:, :] = m - column * scaled_row
            m_ref[:, pl.ds(j, 1), :] = pivot_row / jnp.sqrt(pivot)
            return carry

        lax.fori_loop(0, tile, step, 0)
    m = m_ref[...]
    upper_ref[...] = jnp.where(rows[:, :, :n] <= lanes[:, :, :n], m[:, :, :n], 0.0)
    inv_ref[...] = m[:, :, n:]


def factor(gram):
    freqs, n, _ = gram.shape
    return pl.pallas_call(
        _factor_kernel,
        out_shape=(jax.ShapeDtypeStruct(gram.shape, gram.dtype), jax.ShapeDtypeStruct(gram.shape, gram.dtype)),
        scratch_shapes=[pltpu.VMEM((freqs, n, 2 * n), jnp.float32)],
    )(gram)


def all_sum(x, axes, count):
    pieces = x.reshape(count, x.size // count)
    mine = lax.all_to_all(pieces, axes, 0, 0, tiled=True).sum(0, keepdims=True)
    spread = jnp.broadcast_to(mine, pieces.shape)
    return lax.all_to_all(spread, axes, 0, 0, tiled=True).reshape(x.shape)


def _dft_kernel(core_ref, table_ref, snap_ref, sent_ref, kept_ref):
    chips, a_step, _, pts_dev = kept_ref.shape
    core = core_ref[0]
    res = jnp.dot(table_ref[...], snap_ref[...], precision=lax.Precision.HIGHEST,
                  preferred_element_type=jnp.float32)
    for a in range(a_step):
        for v in range(2 * chips):
            start = (a * 2 * chips + v) * pts_dev
            piece = res[:, start:start + pts_dev]

            @pl.when(core == v % 2)
            def _():
                kept_ref[v // 2, a] = piece

            @pl.when(core != v % 2)
            def _():
                sent_ref[v // 2, a] = piece


def partial_dft(table_t, snapshots, core, n_aa, n_ba):
    a_step = math.gcd(4, n_aa)
    rows, time_dev = table_t.shape
    points = snapshots.shape[1]
    pts_dev = points // (n_aa * n_ba)
    width = a_step * n_ba * pts_dev
    half = pl.BlockSpec((n_ba // 2, a_step, rows, pts_dev), lambda i, c: (0, i, 0, 0))
    shape = jax.ShapeDtypeStruct((n_ba // 2, n_aa, rows, pts_dev), jnp.float32)
    return pl.pallas_call(
        _dft_kernel,
        grid_spec=pltpu.PrefetchScalarGridSpec(
            num_scalar_prefetch=1,
            grid=(n_aa // a_step,),
            in_specs=[
                pl.BlockSpec((rows, time_dev), lambda i, c: (0, 0)),
                pl.BlockSpec((time_dev, width), lambda i, c: (0, i)),
            ],
            out_specs=[half, half],
        ),
        out_shape=(shape, shape),
    )(core, table_t, snapshots)


def sum_over_ba(sent, kept, n_ba):
    u = lax.axis_index("ba")
    cores = 2
    chips = n_ba // cores
    y = u // cores
    chip_sum = kept + lax.ppermute(sent, "ba", [(i, i ^ 1) for i in range(n_ba)])
    total = lax.dynamic_index_in_dim(chip_sum, y, axis=0, keepdims=True)
    for shift in range(1, chips):
        out = lax.dynamic_index_in_dim(chip_sum, (y + shift) % chips, axis=0, keepdims=True)
        perm = [(i, ((i // cores + shift) % chips) * cores + i % cores) for i in range(n_ba)]
        total = total + lax.ppermute(out, "ba", perm)
    return total


def local(snapshots):
    time_dev, points = snapshots.shape
    n_aa = lax.axis_size("aa")
    n_ba = lax.axis_size("ba")
    pts_dev = points // (n_aa * n_ba)
    block_len = time_dev * n_ba
    u = lax.axis_index("ba")
    table = spectral_rows(block_len, points, u * time_dev, time_dev)
    table_t = jnp.transpose(table, (2, 1, 0)).reshape(2 * FREQS, time_dev)
    core = (u % 2).astype(jnp.int32).reshape(1)
    sent, kept = partial_dft(table_t, snapshots, core, n_aa, n_ba)
    block_spec = sum_over_ba(sent, kept, n_ba)
    spectra = lax.all_to_all(block_spec, "aa", split_axis=1, concat_axis=0, tiled=True)
    blocks = spectra.shape[0]
    columns = 2 * blocks
    cols = jnp.transpose(spectra.reshape(blocks, FREQS, 2, pts_dev), (1, 0, 2, 3)).reshape(
        FREQS, columns, pts_dev
    )
    product = jnp.einsum("fip,fjp->fij", cols, cols, precision=lax.Precision.HIGHEST)
    gram_sum = all_sum(product, ("aa", "ba"), n_aa * n_ba)
    upper_factor, inverse = factor(gram_sum)
    pod_modes = math.sqrt(points) * jnp.einsum(
        "fij,fjp->fip", inverse, cols, precision=lax.Precision.HIGHEST
    )
    return (upper_factor, pod_modes)


def solution(mesh):
    placed = (P(("aa", "ba"), None),)
    return jax.shard_map(
        local,
        mesh=mesh,
        in_specs=placed,
        out_specs=(P(), P(None, None, ("aa", "ba"))),
        check_vma=False,
    )
```

```python
import functools
import math

import jax
import jax.numpy as jnp
from jax import lax
from jax.experimental import pallas as pl
from jax.experimental.pallas import tpu as pltpu
from jax.sharding import PartitionSpec as P

FREQS = 8


def spectral_rows(block_len, points, first, count):
    sample = first + jnp.arange(count, dtype=jnp.int32)
    harmonic = jnp.arange(1, FREQS + 1, dtype=jnp.int32)
    phase_turns = (sample[:, None] * harmonic[None, :] % block_len).astype(jnp.float32) * (
        2.0 * math.pi / block_len
    )
    full = jnp.arange(block_len, dtype=jnp.int32).astype(jnp.float32) * (2.0 * math.pi / block_len)
    full_window = 0.5 - 0.5 * jnp.cos(full)
    norm_scale = 1.0 / jnp.sqrt(points * jnp.sum(full_window * full_window))
    sample_angle = sample.astype(jnp.float32) * (2.0 * math.pi / block_len)
    window = 0.5 - 0.5 * jnp.cos(sample_angle)
    cosine = window[:, None] * jnp.cos(phase_turns) * norm_scale
    sine = -window[:, None] * jnp.sin(phase_turns) * norm_scale
    return jnp.stack([cosine, sine], axis=1)


def _factor_kernel(scale, a_ref, cols_ref, upper_ref, modes_ref, m_ref):
    freqs, n, _ = a_ref.shape
    rows = lax.broadcasted_iota(jnp.int32, (freqs, n, 2 * n), 1)
    lanes = lax.broadcasted_iota(jnp.int32, (freqs, n, 2 * n), 2)
    m_ref[...] = jnp.concatenate([a_ref[...], (rows[:, :, :n] == lanes[:, :, :n]).astype(jnp.float32)], axis=2)
    tile = math.gcd(8, n)
    for lo in range(0, n, tile):
        def step(jj, carry, lo=lo):
            j = lo + jj
            m = m_ref[:, lo:, :]
            pivot_row = m_ref[:, pl.ds(j, 1), :]
            pivot = jnp.sum(jnp.where(lanes[:, :1] == j, pivot_row, 0.0), axis=2, keepdims=True)
            scaled_row = pivot_row / pivot
            column = jnp.sum(jnp.where(lanes[:, lo:] == j, m, 0.0), axis=2, keepdims=True)
            column = jnp.where(rows[:, lo:, :1] > j, column, 0.0)
            m_ref[:, lo:, :] = m - column * scaled_row
            m_ref[:, pl.ds(j, 1), :] = pivot_row / jnp.sqrt(pivot)
            return carry

        lax.fori_loop(0, tile, step, 0)
    m = m_ref[...]
    upper_ref[...] = jnp.where(rows[:, :, :n] <= lanes[:, :, :n], m[:, :, :n], 0.0)
    for f in range(freqs):
        modes_ref[f] = scale * jnp.dot(m[f, :, n:], cols_ref[f], precision=lax.Precision.HIGHEST,
                                       preferred_element_type=jnp.float32)


def factor_and_modes(gram, cols, scale):
    freqs, n, _ = gram.shape
    return pl.pallas_call(
        functools.partial(_factor_kernel, scale),
        out_shape=(jax.ShapeDtypeStruct(gram.shape, gram.dtype), jax.ShapeDtypeStruct(cols.shape, cols.dtype)),
        scratch_shapes=[pltpu.VMEM((freqs, n, 2 * n), jnp.float32)],
    )(gram, cols)


def all_sum(x, axes, count):
    pieces = x.reshape(count, x.size // count)
    mine = lax.all_to_all(pieces, axes, 0, 0, tiled=True).sum(0, keepdims=True)
    spread = jnp.broadcast_to(mine, pieces.shape)
    return lax.all_to_all(spread, axes, 0, 0, tiled=True).reshape(x.shape)


def _dft_kernel(core_ref, table_ref, snap_ref, out_ref):
    _, chips, a_step, _, pts_dev = out_ref.shape
    core = core_ref[0]
    res = jnp.dot(table_ref[...], snap_ref[...], precision=lax.Precision.HIGHEST,
                  preferred_element_type=jnp.float32)
    for a in range(a_step):
        for v in range(2 * chips):
            cv = v % 2
            keep = 1 - (cv + core - 2 * cv * core)
            start = (a * 2 * chips + v) * pts_dev
            out_ref[keep, v // 2, a] = res[:, start:start + pts_dev]


def partial_dft(table_t, snapshots, core, n_aa, n_ba):
    a_step = math.gcd(4, n_aa)
    rows, time_dev = table_t.shape
    points = snapshots.shape[1]
    pts_dev = points // (n_aa * n_ba)
    width = a_step * n_ba * pts_dev
    return pl.pallas_call(
        _dft_kernel,
        grid_spec=pltpu.PrefetchScalarGridSpec(
            num_scalar_prefetch=1,
            grid=(n_aa // a_step,),
            in_specs=[
                pl.BlockSpec((rows, time_dev), lambda i, c: (0, 0)),
                pl.BlockSpec((time_dev, width), lambda i, c: (0, i)),
            ],
            out_specs=pl.BlockSpec((2, n_ba // 2, a_step, rows, pts_dev), lambda i, c: (0, 0, i, 0, 0)),
        ),
        out_shape=jax.ShapeDtypeStruct((2, n_ba // 2, n_aa, rows, pts_dev), jnp.float32),
    )(core, table_t, snapshots)


def sum_over_ba(partial, n_ba):
    u = lax.axis_index("ba")
    cores = 2
    chips = n_ba // cores
    y = u // cores
    chip_sum = partial[1] + lax.ppermute(partial[0], "ba", [(i, i ^ 1) for i in range(n_ba)])
    total = lax.dynamic_index_in_dim(chip_sum, y, axis=0, keepdims=True)
    for shift in range(1, chips):
        out = lax.dynamic_index_in_dim(chip_sum, (y + shift) % chips, axis=0, keepdims=True)
        perm = [(i, ((i // cores + shift) % chips) * cores + i % cores) for i in range(n_ba)]
        total = total + lax.ppermute(out, "ba", perm)
    return total


def local(snapshots):
    time_dev, points = snapshots.shape
    n_aa = lax.axis_size("aa")
    n_ba = lax.axis_size("ba")
    pts_dev = points // (n_aa * n_ba)
    block_len = time_dev * n_ba
    u = lax.axis_index("ba")
    table = spectral_rows(block_len, points, u * time_dev, time_dev)
    table_t = jnp.transpose(table, (2, 1, 0)).reshape(2 * FREQS, time_dev)
    core = (u % 2).astype(jnp.int32).reshape(1)
    partial = partial_dft(table_t, snapshots, core, n_aa, n_ba)
    block_spec = sum_over_ba(partial, n_ba)
    spectra = lax.all_to_all(block_spec, "aa", split_axis=1, concat_axis=0, tiled=True)
    blocks = spectra.shape[0]
    columns = 2 * blocks
    cols = jnp.transpose(spectra.reshape(blocks, FREQS, 2, pts_dev), (1, 0, 2, 3)).reshape(
        FREQS, columns, pts_dev
    )
    product = jnp.einsum("fip,fjp->fij", cols, cols, precision=lax.Precision.HIGHEST)
    gram_sum = all_sum(product, ("aa", "ba"), n_aa * n_ba)
    upper_factor, pod_modes = factor_and_modes(gram_sum, cols, math.sqrt(points))
    return (upper_factor, pod_modes)


def solution(mesh):
    placed = (P(("aa", "ba"), None),)
    return jax.shard_map(
        local,
        mesh=mesh,
        in_specs=placed,
        out_specs=(P(), P(None, None, ("aa", "ba"))),
        check_vma=False,
    )
```

```python
import functools
import math

import jax
import jax.numpy as jnp
from jax import lax
from jax.experimental import pallas as pl
from jax.experimental.pallas import tpu as pltpu
from jax.sharding import PartitionSpec as P

FREQS = 8


def spectral_rows(block_len, points, first, count):
    sample = first + jnp.arange(count, dtype=jnp.int32)
    harmonic = jnp.arange(1, FREQS + 1, dtype=jnp.int32)
    phase_turns = (sample[:, None] * harmonic[None, :] % block_len).astype(jnp.float32) * (
        2.0 * math.pi / block_len
    )
    full = jnp.arange(block_len, dtype=jnp.int32).astype(jnp.float32) * (2.0 * math.pi / block_len)
    full_window = 0.5 - 0.5 * jnp.cos(full)
    norm_scale = 1.0 / jnp.sqrt(points * jnp.sum(full_window * full_window))
    sample_angle = sample.astype(jnp.float32) * (2.0 * math.pi / block_len)
    window = 0.5 - 0.5 * jnp.cos(sample_angle)
    cosine = window[:, None] * jnp.cos(phase_turns) * norm_scale
    sine = -window[:, None] * jnp.sin(phase_turns) * norm_scale
    return jnp.stack([cosine, sine], axis=1)


def _factor_kernel(scale, a_ref, cols_ref, upper_ref, modes_ref, m_ref):
    freqs, n, _ = a_ref.shape
    rows = lax.broadcasted_iota(jnp.int32, (freqs, n, 2 * n), 1)
    lanes = lax.broadcasted_iota(jnp.int32, (freqs, n, 2 * n), 2)
    m_ref[...] = jnp.concatenate([a_ref[...], (rows[:, :, :n] == lanes[:, :, :n]).astype(jnp.float32)], axis=2)
    tile = math.gcd(8, n)
    for lo in range(0, n, tile):
        def step(jj, carry, lo=lo):
            j = lo + jj
            m = m_ref[:, lo:, :]
            pivot_row = m_ref[:, pl.ds(j, 1), :]
            pivot = jnp.sum(jnp.where(lanes[:, :1] == j, pivot_row, 0.0), axis=2, keepdims=True)
            scaled_row = pivot_row / pivot
            column = jnp.sum(jnp.where(lanes[:, lo:] == j, m, 0.0), axis=2, keepdims=True)
            column = jnp.where(rows[:, lo:, :1] > j, column, 0.0)
            m_ref[:, lo:, :] = m - column * scaled_row
            m_ref[:, pl.ds(j, 1), :] = pivot_row / jnp.sqrt(pivot)
            return carry

        lax.fori_loop(0, tile, step, 0)
    m = m_ref[...]
    upper_ref[...] = jnp.where(rows[:, :, :n] <= lanes[:, :, :n], m[:, :, :n], 0.0)
    for f in range(freqs):
        modes_ref[f] = scale * jnp.dot(m[f, :, n:], cols_ref[f], precision=lax.Precision.HIGHEST,
                                       preferred_element_type=jnp.float32)


def factor_and_modes(gram, cols, scale):
    freqs, n, _ = gram.shape
    return pl.pallas_call(
        functools.partial(_factor_kernel, scale),
        out_shape=(jax.ShapeDtypeStruct(gram.shape, gram.dtype), jax.ShapeDtypeStruct(cols.shape, cols.dtype)),
        scratch_shapes=[pltpu.VMEM((freqs, n, 2 * n), jnp.float32)],
    )(gram, cols)


def all_sum(x, axes, count):
    pieces = x.reshape(count, x.size // count)
    mine = lax.all_to_all(pieces, axes, 0, 0, tiled=True).sum(0, keepdims=True)
    spread = jnp.broadcast_to(mine, pieces.shape)
    return lax.all_to_all(spread, axes, 0, 0, tiled=True).reshape(x.shape)


def _dft_kernel(core_ref, table_ref, snap_ref, out_ref):
    _, chips, a_step, _, pts_dev = out_ref.shape
    core = core_ref[0]
    res = jnp.dot(table_ref[...], snap_ref[...], precision=lax.Precision.HIGHEST,
                  preferred_element_type=jnp.float32)
    for a in range(a_step):
        for v in range(2 * chips):
            cv = v % 2
            keep = 1 - (cv + core - 2 * cv * core)
            start = (a * 2 * chips + v) * pts_dev
            out_ref[keep, v // 2, a] = res[:, start:start + pts_dev]


def partial_dft(table_t, snapshots, core, n_aa, n_ba):
    a_step = math.gcd(8, n_aa)
    rows, time_dev = table_t.shape
    points = snapshots.shape[1]
    pts_dev = points // (n_aa * n_ba)
    width = a_step * n_ba * pts_dev
    return pl.pallas_call(
        _dft_kernel,
        grid_spec=pltpu.PrefetchScalarGridSpec(
            num_scalar_prefetch=1,
            grid=(n_aa // a_step,),
            in_specs=[
                pl.BlockSpec((rows, time_dev), lambda i, c: (0, 0)),
                pl.BlockSpec((time_dev, width), lambda i, c: (0, i)),
            ],
            out_specs=pl.BlockSpec((2, n_ba // 2, a_step, rows, pts_dev), lambda i, c: (0, 0, i, 0, 0)),
        ),
        out_shape=jax.ShapeDtypeStruct((2, n_ba // 2, n_aa, rows, pts_dev), jnp.float32),
    )(core, table_t, snapshots)


def sum_over_ba(partial, n_ba):
    u = lax.axis_index("ba")
    cores = 2
    chips = n_ba // cores
    y = u // cores
    chip_sum = partial[1] + lax.ppermute(partial[0], "ba", [(i, i ^ 1) for i in range(n_ba)])
    total = lax.dynamic_index_in_dim(chip_sum, y, axis=0, keepdims=True)
    for shift in range(1, chips):
        out = lax.dynamic_index_in_dim(chip_sum, (y + shift) % chips, axis=0, keepdims=True)
        perm = [(i, ((i // cores + shift) % chips) * cores + i % cores) for i in range(n_ba)]
        total = total + lax.ppermute(out, "ba", perm)
    return total


def local(snapshots):
    time_dev, points = snapshots.shape
    n_aa = lax.axis_size("aa")
    n_ba = lax.axis_size("ba")
    pts_dev = points // (n_aa * n_ba)
    block_len = time_dev * n_ba
    u = lax.axis_index("ba")
    table = spectral_rows(block_len, points, u * time_dev, time_dev)
    table_t = jnp.transpose(table, (2, 1, 0)).reshape(2 * FREQS, time_dev)
    core = (u % 2).astype(jnp.int32).reshape(1)
    partial = partial_dft(table_t, snapshots, core, n_aa, n_ba)
    block_spec = sum_over_ba(partial, n_ba)
    spectra = lax.all_to_all(block_spec, "aa", split_axis=1, concat_axis=0, tiled=True)
    blocks = spectra.shape[0]
    columns = 2 * blocks
    cols = jnp.transpose(spectra.reshape(blocks, FREQS, 2, pts_dev), (1, 0, 2, 3)).reshape(
        FREQS, columns, pts_dev
    )
    product = jnp.einsum("fip,fjp->fij", cols, cols, precision=lax.Precision.HIGHEST)
    gram_sum = all_sum(product, ("aa", "ba"), n_aa * n_ba)
    upper_factor, pod_modes = factor_and_modes(gram_sum, cols, math.sqrt(points))
    return (upper_factor, pod_modes)


def solution(mesh):
    placed = (P(("aa", "ba"), None),)
    return jax.shard_map(
        local,
        mesh=mesh,
        in_specs=placed,
        out_specs=(P(), P(None, None, ("aa", "ba"))),
        check_vma=False,
    )
```

```python
import functools
import math

import jax
import jax.numpy as jnp
from jax import lax
from jax.experimental import pallas as pl
from jax.experimental.pallas import tpu as pltpu
from jax.sharding import PartitionSpec as P

FREQS = 8


def spectral_rows(block_len, points, first, count):
    sample = first + jnp.arange(count, dtype=jnp.int32)
    harmonic = jnp.arange(1, FREQS + 1, dtype=jnp.int32)
    phase_turns = (sample[:, None] * harmonic[None, :] % block_len).astype(jnp.float32) * (
        2.0 * math.pi / block_len
    )
    full = jnp.arange(block_len, dtype=jnp.int32).astype(jnp.float32) * (2.0 * math.pi / block_len)
    full_window = 0.5 - 0.5 * jnp.cos(full)
    norm_scale = 1.0 / jnp.sqrt(points * jnp.sum(full_window * full_window))
    sample_angle = sample.astype(jnp.float32) * (2.0 * math.pi / block_len)
    window = 0.5 - 0.5 * jnp.cos(sample_angle)
    cosine = window[:, None] * jnp.cos(phase_turns) * norm_scale
    sine = -window[:, None] * jnp.sin(phase_turns) * norm_scale
    return jnp.stack([cosine, sine], axis=1)


def _factor_kernel(scale, a_ref, cols_ref, upper_ref, modes_ref, m_ref):
    freqs, n, _ = a_ref.shape
    rows = lax.broadcasted_iota(jnp.int32, (freqs, n, 2 * n), 1)
    lanes = lax.broadcasted_iota(jnp.int32, (freqs, n, 2 * n), 2)
    m_ref[...] = jnp.concatenate([a_ref[...], (rows[:, :, :n] == lanes[:, :, :n]).astype(jnp.float32)], axis=2)
    tile = math.gcd(8, n)
    for lo in range(0, n, tile):
        def step(jj, carry, lo=lo):
            j = lo + jj
            m = m_ref[:, lo:, :]
            pivot_row = m_ref[:, pl.ds(j, 1), :]
            pivot = jnp.sum(jnp.where(lanes[:, :1] == j, pivot_row, 0.0), axis=2, keepdims=True)
            scaled_row = pivot_row / pivot
            column = jnp.sum(jnp.where(lanes[:, lo:] == j, m, 0.0), axis=2, keepdims=True)
            column = jnp.where(rows[:, lo:, :1] > j, column, 0.0)
            m_ref[:, lo:, :] = m - column * scaled_row
            m_ref[:, pl.ds(j, 1), :] = pivot_row / jnp.sqrt(pivot)
            return carry

        lax.fori_loop(0, tile, step, 0)
    m = m_ref[...]
    upper_ref[...] = jnp.where(rows[:, :, :n] <= lanes[:, :, :n], m[:, :, :n], 0.0)
    for f in range(freqs):
        modes_ref[f] = scale * jnp.dot(m[f, :, n:], cols_ref[f], precision=lax.Precision.HIGHEST,
                                       preferred_element_type=jnp.float32)


def factor_and_modes(gram, cols, scale):
    freqs, n, _ = gram.shape
    return pl.pallas_call(
        functools.partial(_factor_kernel, scale),
        out_shape=(jax.ShapeDtypeStruct(gram.shape, gram.dtype), jax.ShapeDtypeStruct(cols.shape, cols.dtype)),
        scratch_shapes=[pltpu.VMEM((freqs, n, 2 * n), jnp.float32)],
    )(gram, cols)


def all_sum(x, axes, count):
    pieces = x.reshape(count, x.size // count)
    mine = lax.all_to_all(pieces, axes, 0, 0, tiled=True).sum(0, keepdims=True)
    spread = jnp.broadcast_to(mine, pieces.shape)
    return lax.all_to_all(spread, axes, 0, 0, tiled=True).reshape(x.shape)


def _dft_kernel(core_ref, table_ref, snap_ref, out_ref):
    _, chips, a_step, _, pts_dev = out_ref.shape
    core = core_ref[0]
    res = jnp.dot(table_ref[...], snap_ref[...], precision=lax.Precision.HIGHEST,
                  preferred_element_type=jnp.float32)
    for a in range(a_step):
        for v in range(2 * chips):
            cv = v % 2
            keep = 1 - (cv + core - 2 * cv * core)
            start = (a * 2 * chips + v) * pts_dev
            out_ref[keep, v // 2, a] = res[:, start:start + pts_dev]


def partial_dft(table_t, snapshots, core, n_aa, n_ba):
    a_step = math.gcd(16, n_aa)
    rows, time_dev = table_t.shape
    points = snapshots.shape[1]
    pts_dev = points // (n_aa * n_ba)
    width = a_step * n_ba * pts_dev
    return pl.pallas_call(
        _dft_kernel,
        grid_spec=pltpu.PrefetchScalarGridSpec(
            num_scalar_prefetch=1,
            grid=(n_aa // a_step,),
            in_specs=[
                pl.BlockSpec((rows, time_dev), lambda i, c: (0, 0)),
                pl.BlockSpec((time_dev, width), lambda i, c: (0, i)),
            ],
            out_specs=pl.BlockSpec((2, n_ba // 2, a_step, rows, pts_dev), lambda i, c: (0, 0, i, 0, 0)),
        ),
        out_shape=jax.ShapeDtypeStruct((2, n_ba // 2, n_aa, rows, pts_dev), jnp.float32),
    )(core, table_t, snapshots)


def sum_over_ba(partial, n_ba):
    u = lax.axis_index("ba")
    cores = 2
    chips = n_ba // cores
    y = u // cores
    chip_sum = partial[1] + lax.ppermute(partial[0], "ba", [(i, i ^ 1) for i in range(n_ba)])
    total = lax.dynamic_index_in_dim(chip_sum, y, axis=0, keepdims=True)
    for shift in range(1, chips):
        out = lax.dynamic_index_in_dim(chip_sum, (y + shift) % chips, axis=0, keepdims=True)
        perm = [(i, ((i // cores + shift) % chips) * cores + i % cores) for i in range(n_ba)]
        total = total + lax.ppermute(out, "ba", perm)
    return total


def local(snapshots):
    time_dev, points = snapshots.shape
    n_aa = lax.axis_size("aa")
    n_ba = lax.axis_size("ba")
    pts_dev = points // (n_aa * n_ba)
    block_len = time_dev * n_ba
    u = lax.axis_index("ba")
    table = spectral_rows(block_len, points, u * time_dev, time_dev)
    table_t = jnp.transpose(table, (2, 1, 0)).reshape(2 * FREQS, time_dev)
    core = (u % 2).astype(jnp.int32).reshape(1)
    partial = partial_dft(table_t, snapshots, core, n_aa, n_ba)
    block_spec = sum_over_ba(partial, n_ba)
    spectra = lax.all_to_all(block_spec, "aa", split_axis=1, concat_axis=0, tiled=True)
    blocks = spectra.shape[0]
    columns = 2 * blocks
    cols = jnp.transpose(spectra.reshape(blocks, FREQS, 2, pts_dev), (1, 0, 2, 3)).reshape(
        FREQS, columns, pts_dev
    )
    product = jnp.einsum("fip,fjp->fij", cols, cols, precision=lax.Precision.HIGHEST)
    gram_sum = all_sum(product, ("aa", "ba"), n_aa * n_ba)
    upper_factor, pod_modes = factor_and_modes(gram_sum, cols, math.sqrt(points))
    return (upper_factor, pod_modes)


def solution(mesh):
    placed = (P(("aa", "ba"), None),)
    return jax.shard_map(
        local,
        mesh=mesh,
        in_specs=placed,
        out_specs=(P(), P(None, None, ("aa", "ba"))),
        check_vma=False,
    )
```

```python
import functools
import math

import jax
import jax.numpy as jnp
from jax import lax
from jax.experimental import pallas as pl
from jax.experimental.pallas import tpu as pltpu
from jax.sharding import PartitionSpec as P

FREQS = 8


def spectral_rows(block_len, points, first, count):
    sample = first + jnp.arange(count, dtype=jnp.int32)
    harmonic = jnp.arange(1, FREQS + 1, dtype=jnp.int32)
    phase_turns = (sample[:, None] * harmonic[None, :] % block_len).astype(jnp.float32) * (
        2.0 * math.pi / block_len
    )
    full = jnp.arange(block_len, dtype=jnp.int32).astype(jnp.float32) * (2.0 * math.pi / block_len)
    full_window = 0.5 - 0.5 * jnp.cos(full)
    norm_scale = 1.0 / jnp.sqrt(points * jnp.sum(full_window * full_window))
    sample_angle = sample.astype(jnp.float32) * (2.0 * math.pi / block_len)
    window = 0.5 - 0.5 * jnp.cos(sample_angle)
    cosine = window[:, None] * jnp.cos(phase_turns) * norm_scale
    sine = -window[:, None] * jnp.sin(phase_turns) * norm_scale
    return jnp.stack([cosine, sine], axis=1)


def _factor_kernel(scale, a_ref, cols_ref, upper_ref, modes_ref, m_ref):
    freqs, half, _ = a_ref.shape
    n = 2 * half
    rows = lax.broadcasted_iota(jnp.int32, (freqs, n, 2 * n), 1)
    lanes = lax.broadcasted_iota(jnp.int32, (freqs, n, 2 * n), 2)
    packed = a_ref[...]
    left = jnp.concatenate([packed[:, r // 2:r // 2 + 1, (r % 2) * n:(r % 2 + 1) * n] for r in range(n)], axis=1)
    m_ref[...] = jnp.concatenate([left, (rows[:, :, :n] == lanes[:, :, :n]).astype(jnp.float32)], axis=2)
    tile = math.gcd(8, n)
    for lo in range(0, n, tile):
        def step(jj, carry, lo=lo):
            j = lo + jj
            m = m_ref[:, lo:, :]
            pivot_row = m_ref[:, pl.ds(j, 1), :]
            pivot = jnp.sum(jnp.where(lanes[:, :1] == j, pivot_row, 0.0), axis=2, keepdims=True)
            scaled_row = pivot_row / pivot
            column = jnp.sum(jnp.where(lanes[:, lo:] == j, m, 0.0), axis=2, keepdims=True)
            column = jnp.where(rows[:, lo:, :1] > j, column, 0.0)
            m_ref[:, lo:, :] = m - column * scaled_row
            m_ref[:, pl.ds(j, 1), :] = pivot_row / jnp.sqrt(pivot)
            return carry

        lax.fori_loop(0, tile, step, 0)
    m = m_ref[...]
    upper_ref[...] = jnp.where(rows[:, :, :n] <= lanes[:, :, :n], m[:, :, :n], 0.0)
    for f in range(freqs):
        modes_ref[f] = scale * jnp.dot(m[f, :, n:], cols_ref[f], precision=lax.Precision.HIGHEST,
                                       preferred_element_type=jnp.float32)


def factor_and_modes(gram, cols, scale):
    freqs, n, _ = gram.shape
    return pl.pallas_call(
        functools.partial(_factor_kernel, scale),
        out_shape=(jax.ShapeDtypeStruct(gram.shape, gram.dtype), jax.ShapeDtypeStruct(cols.shape, cols.dtype)),
        scratch_shapes=[pltpu.VMEM((freqs, n, 2 * n), jnp.float32)],
    )(gram.reshape(freqs, n // 2, 2 * n), cols)


def all_sum(x, axes, count):
    pieces = x.reshape(count, x.size // count)
    mine = lax.all_to_all(pieces, axes, 0, 0, tiled=True).sum(0, keepdims=True)
    spread = jnp.broadcast_to(mine, pieces.shape)
    return lax.all_to_all(spread, axes, 0, 0, tiled=True).reshape(x.shape)


def _dft_kernel(core_ref, table_ref, snap_ref, out_ref):
    _, chips, a_step, _, pts_dev = out_ref.shape
    core = core_ref[0]
    res = jnp.dot(table_ref[...], snap_ref[...], precision=lax.Precision.HIGHEST,
                  preferred_element_type=jnp.float32)
    for a in range(a_step):
        for v in range(2 * chips):
            cv = v % 2
            keep = 1 - (cv + core - 2 * cv * core)
            start = (a * 2 * chips + v) * pts_dev
            out_ref[keep, v // 2, a] = res[:, start:start + pts_dev]


def partial_dft(table_t, snapshots, core, n_aa, n_ba):
    a_step = math.gcd(8, n_aa)
    rows, time_dev = table_t.shape
    points = snapshots.shape[1]
    pts_dev = points // (n_aa * n_ba)
    width = a_step * n_ba * pts_dev
    return pl.pallas_call(
        _dft_kernel,
        grid_spec=pltpu.PrefetchScalarGridSpec(
            num_scalar_prefetch=1,
            grid=(n_aa // a_step,),
            in_specs=[
                pl.BlockSpec((rows, time_dev), lambda i, c: (0, 0)),
                pl.BlockSpec((time_dev, width), lambda i, c: (0, i)),
            ],
            out_specs=pl.BlockSpec((2, n_ba // 2, a_step, rows, pts_dev), lambda i, c: (0, 0, i, 0, 0)),
        ),
        out_shape=jax.ShapeDtypeStruct((2, n_ba // 2, n_aa, rows, pts_dev), jnp.float32),
    )(core, table_t, snapshots)


def sum_over_ba(partial, n_ba):
    u = lax.axis_index("ba")
    cores = 2
    chips = n_ba // cores
    y = u // cores
    chip_sum = partial[1] + lax.ppermute(partial[0], "ba", [(i, i ^ 1) for i in range(n_ba)])
    total = lax.dynamic_index_in_dim(chip_sum, y, axis=0, keepdims=True)
    for shift in range(1, chips):
        out = lax.dynamic_index_in_dim(chip_sum, (y + shift) % chips, axis=0, keepdims=True)
        perm = [(i, ((i // cores + shift) % chips) * cores + i % cores) for i in range(n_ba)]
        total = total + lax.ppermute(out, "ba", perm)
    return total


def local(snapshots):
    time_dev, points = snapshots.shape
    n_aa = lax.axis_size("aa")
    n_ba = lax.axis_size("ba")
    pts_dev = points // (n_aa * n_ba)
    block_len = time_dev * n_ba
    u = lax.axis_index("ba")
    table = spectral_rows(block_len, points, u * time_dev, time_dev)
    table_t = jnp.transpose(table, (2, 1, 0)).reshape(2 * FREQS, time_dev)
    core = (u % 2).astype(jnp.int32).reshape(1)
    partial = partial_dft(table_t, snapshots, core, n_aa, n_ba)
    block_spec = sum_over_ba(partial, n_ba)
    spectra = lax.all_to_all(block_spec, "aa", split_axis=1, concat_axis=0, tiled=True)
    blocks = spectra.shape[0]
    columns = 2 * blocks
    cols = jnp.transpose(spectra.reshape(blocks, FREQS, 2, pts_dev), (1, 0, 2, 3)).reshape(
        FREQS, columns, pts_dev
    )
    product = jnp.einsum("fip,fjp->fij", cols, cols, precision=lax.Precision.HIGHEST)
    gram_sum = all_sum(product, ("aa", "ba"), n_aa * n_ba)
    upper_factor, pod_modes = factor_and_modes(gram_sum, cols, math.sqrt(points))
    return (upper_factor, pod_modes)


def solution(mesh):
    placed = (P(("aa", "ba"), None),)
    return jax.shard_map(
        local,
        mesh=mesh,
        in_specs=placed,
        out_specs=(P(), P(None, None, ("aa", "ba"))),
        check_vma=False,
    )
```
